32 devices in a mesh: dom: 4 (over x, core), fsdp: 8 (over z, y).
Axes of the slice: x: 2, y: 2, z: 4, core: 2. Of those that a mesh axis runs over, the one named last changes fastest.
Arguments:
- acts: bfloat16 [4096, 14336], P(('dom', 'fsdp')), may hold values from -24 to 24
- cotangent: bfloat16 [4096, 4096], P(('dom', 'fsdp')), may hold values from -0.75 to 0.75
- weight: bfloat16 [14336, 4096], P(('dom', 'fsdp')), may hold values from -0.046875 to 0.046875
- moment: float32 [14336, 4096], P(('dom', 'fsdp')), may hold values from -6 to 6
- second: float32 [14336, 4096], P(('dom', 'fsdp')), may hold values from 0.3 to 3
- log_weights: float32 [4], replicated, may hold values from -1 to 1
- domain_ids: int32 [4], replicated, may hold values from 0 to 3, each once
- step_count: int32 [1], replicated, may hold values from 1 to 8
Outputs:
- new_weight: bfloat16 [14336, 4096], P(('dom', 'fsdp'))
- new_moment: float32 [14336, 4096], P(('dom', 'fsdp'))
- new_second: float32 [14336, 4096], P(('dom', 'fsdp'))
- new_domain_weights: float32 [4], replicated
The draws below stay inside these ranges and needn't reach their ends.
All inputs are finite; a program needn't handle non-finite values.
Results may differ from the reference program's by a relative error of at most 0.001.
Values may be sent and summed in bfloat16 or wider, within the bound.
No kernel may reach another device: no remote copies, remote signals or barrier semaphores. Data moves between devices by JAX's collectives and lax.ppermute only.
A program may use at most 192 MiB of HBM per device.

```python
import math
import jax
import jax.numpy as jnp
from jax import lax

D = 4096
FF = 14336
DOMS = 4
TOK_GROUP = 1024
TOKENS = 4096


def draw_acts(key, part):
    key_shared, key_own, key_mix, key_block, key_rough = jax.random.split(key, 5)
    shared = jnp.clip(jax.random.normal(key_shared, (TOK_GROUP, FF), jnp.float32), -5.0, 5.0)
    private = jnp.clip(jax.random.normal(key_own, (DOMS, TOK_GROUP, FF), jnp.float32), -5.0, 5.0)
    mixing = jax.random.uniform(key_mix, (DOMS,), jnp.float32, 0.4, 0.8)
    blended = jnp.sqrt(mixing)[:, None, None] * shared[None, :, :] + jnp.sqrt(1.0 - mixing)[:, None, None] * private
    block_log = jax.random.uniform(key_block, (DOMS, 16), jnp.float32, -0.8, 0.8)
    column_log = jnp.repeat(block_log, FF // 16, axis=1)
    rough_log = jax.random.uniform(key_rough, (DOMS, FF), jnp.float32, -0.35, 0.35)
    incline = 0.55 * (2.0 * jnp.arange(FF, dtype=jnp.float32) / (FF - 1) - 1.0)
    column_scale = jnp.exp(column_log + rough_log + incline[None, :])
    scaled = blended * column_scale[:, None, :]
    return jnp.clip(scaled.reshape(TOKENS, FF), -24.0, 24.0).astype(jnp.bfloat16)


def draw_cotangent(key, part):
    key_shared, key_own, key_mix, key_group, key_rows = jax.random.split(key, 5)
    shared = jnp.clip(jax.random.normal(key_shared, (TOK_GROUP, D), jnp.float32), -5.0, 5.0)
    private = jnp.clip(jax.random.normal(key_own, (DOMS, TOK_GROUP, D), jnp.float32), -5.0, 5.0)
    mixing = jax.random.uniform(key_mix, (DOMS,), jnp.float32, 0.4, 0.8)
    blended = jnp.sqrt(mixing)[:, None, None] * shared[None, :, :] + jnp.sqrt(1.0 - mixing)[:, None, None] * private
    group_scale = jnp.exp(jax.random.uniform(key_group, (DOMS,), jnp.float32, -0.8, 0.8))
    row_scale = jnp.exp(jax.random.uniform(key_rows, (TOK_GROUP,), jnp.float32, -1.15, 1.15))
    values = blended * group_scale[:, None, None] * row_scale[None, :, None] / 64.0
    return jnp.clip(values.reshape(TOKENS, D), -0.75, 0.75).astype(jnp.bfloat16)


def levels(own_key, dims, cuts, smallest, top_value):
    gain, own = 1.0, jax.random.fold_in(own_key, 6)
    for position, parts in cuts:
        draws = jnp.exp(jax.random.uniform(jax.random.fold_in(own, position), (parts,), jnp.float32, smallest / len(cuts), top_value / len(cuts)))
        gain = gain * jnp.repeat(draws, dims[position] // parts).reshape([-1 if axis == position else 1 for axis in range(len(dims))])
    return gain


def scatter_about(key, extent, scale, limit, cuts=(), held_as=jnp.bfloat16):
    gain = levels(key, extent, cuts, -0.22, 0.18) if cuts else 1.0
    entries = jax.random.normal(key, extent, jnp.float32) * scale * gain
    return jnp.minimum(jnp.maximum(entries, -limit), limit).astype(held_as)


def setup_inputs(seed: int = 0) -> dict:
    splits = jax.random.split(jax.random.key(seed), 9)
    acts = draw_acts(jax.random.fold_in(splits[8], 71), 0)
    cotangent = draw_cotangent(jax.random.fold_in(splits[8], 71), 0)
    weight = scatter_about(splits[2], (FF, D), FF ** -0.5, 0.046875, ((0, 32),))
    moment = scatter_about(splits[3], (FF, D), 1.0, 6.0, ((0, 32),), jnp.float32)
    second = jnp.clip(jnp.exp(math.log(3.0) - 2.3025851 * jax.random.uniform(splits[4], (FF, D), jnp.float32) ** levels(splits[4], (FF, D), ((0, 32),), -0.2, 0.2)), 0.3, 3.0)
    log_weights = jnp.clip(jax.random.uniform(splits[5], (DOMS,), jnp.float32, -1.0, 1.0), -1.0, 1.0)
    domain_ids = jax.random.permutation(splits[6], DOMS).astype(jnp.int32)
    step_count = jax.random.randint(splits[7], (1,), 1, 9).astype(jnp.int32)
    return dict(acts=acts, cotangent=cotangent, weight=weight, moment=moment, second=second, log_weights=log_weights, domain_ids=domain_ids, step_count=step_count)


def reference(acts, cotangent, weight, moment, second, log_weights, domain_ids, step_count):
    grads = []
    for group in range(DOMS):
        rows_a = acts[group * TOK_GROUP:(group + 1) * TOK_GROUP]
        rows_c = cotangent[group * TOK_GROUP:(group + 1) * TOK_GROUP]
        product = lax.dot_general(rows_a, rows_c, (((0,), (0,)), ((), ())), preferred_element_type=jnp.float32)
        grads.append(product.astype(jnp.bfloat16))
    stacked = jnp.stack(grads)
    block = math.gcd(FF, 1024)
    gram = jnp.zeros((DOMS, DOMS), jnp.float32)
    for begin in range(0, FF, block):
        piece = stacked[:, begin:begin + block].astype(jnp.float32).reshape(DOMS, -1)
        gram = gram + jnp.dot(piece, piece.T, precision=lax.Precision.HIGHEST)
    score = lax.optimization_barrier(jnp.sum(gram, axis=1)) * (DOMS / jnp.trace(gram))
    onehot = (domain_ids[:, None] == jnp.arange(DOMS, dtype=jnp.int32)[None, :]).astype(jnp.float32)
    logits = log_weights + 2.0 * lax.optimization_barrier(jnp.sum(onehot * score[:, None], axis=0))
    new_domain_weights = jax.nn.softmax(logits)
    group_w = lax.optimization_barrier(jnp.sum(onehot * new_domain_weights[None, :], axis=1))
    combined = jnp.zeros((FF, D), jnp.float32)
    for group in range(DOMS):
        combined = combined + group_w[group] * stacked[group].astype(jnp.float32)
    steps_f = step_count[0].astype(jnp.float32)
    new_moment = 0.9 * moment + 0.1 * combined
    new_second = 0.95 * second + 0.05 * combined * combined
    fix_one = 1.0 - jnp.exp(steps_f * jnp.log(jnp.float32(0.9)))
    fix_two = 1.0 - jnp.exp(steps_f * jnp.log(jnp.float32(0.95)))
    update = new_moment / fix_one / (jnp.sqrt(new_second / fix_two) + 1e-08)
    new_weight = (weight.astype(jnp.float32) - 0.002 * update).astype(jnp.bfloat16)
    return (new_weight, new_moment, new_second, new_domain_weights)
```

```python
import jax
import jax.numpy as jnp
from jax import lax
from jax.sharding import PartitionSpec as P

ALL = ("dom", "fsdp")


def on_device(acts, cotangent, weight, moment, second, log_weights, domain_ids, step_count):
    groups = lax.axis_size("dom")
    devices = lax.axis_size(ALL)
    tok_rows = acts.shape[0]
    width = cotangent.shape[1]
    own_rows = weight.shape[0]
    shaped = acts.reshape(tok_rows, devices, own_rows)
    columns = lax.all_to_all(shaped, ALL, split_axis=1, concat_axis=0, tiled=True)
    columns = columns.reshape(groups, devices // groups * tok_rows, own_rows)
    gathered = lax.all_gather(cotangent, ALL, axis=0, tiled=True)
    gathered = gathered.reshape(groups, devices // groups * tok_rows, width)
    owned = lax.dot_general(
        columns, gathered, (((1,), (1,)), ((0,), (0,))), preferred_element_type=jnp.float32
    ).astype(jnp.bfloat16)
    local_gram = jnp.einsum("krd,jrd->kj", owned, owned, preferred_element_type=jnp.float32)
    gram = lax.psum(local_gram, ALL)
    score = jnp.sum(gram, axis=1) * (groups / jnp.trace(gram))
    onehot = (domain_ids[:, None] == jnp.arange(groups, dtype=jnp.int32)[None, :]).astype(
        jnp.float32
    )
    logits = log_weights + 2.0 * jnp.sum(onehot * score[:, None], axis=0)
    new_domain_weights = jax.nn.softmax(logits)
    group_w = jnp.sum(onehot * new_domain_weights[None, :], axis=1)
    combined = jnp.zeros((own_rows, width), jnp.float32)
    for group in range(groups):
        combined = combined + group_w[group] * owned[group].astype(jnp.float32)
    steps_f = step_count[0].astype(jnp.float32)
    new_moment = 0.9 * moment + 0.1 * combined
    new_second = 0.95 * second + 0.05 * combined * combined
    fix_one = 1.0 - jnp.exp(steps_f * jnp.log(jnp.float32(0.9)))
    fix_two = 1.0 - jnp.exp(steps_f * jnp.log(jnp.float32(0.95)))
    update = new_moment / fix_one / (jnp.sqrt(new_second / fix_two) + 1e-08)
    new_weight = (weight.astype(jnp.float32) - 0.002 * update).astype(jnp.bfloat16)
    return (new_weight, new_moment, new_second, new_domain_weights)


def solution(mesh):
    return jax.shard_map(
        on_device,
        mesh=mesh,
        in_specs=(
            P(ALL, None),
            P(ALL, None),
            P(ALL, None),
            P(ALL, None),
            P(ALL, None),
            P(),
            P(),
            P(),
        ),
        out_specs=(
            P(ALL, None),
            P(ALL, None),
            P(ALL, None),
            P(),
        ),
        check_vma=False,
    )
```

```python
import jax
import jax.numpy as jnp
from jax import lax
from jax.sharding import Mesh, PartitionSpec as P

FLAT = ("x", "core", "fsdp")


def on_device(acts, cotangent, weight, moment, second, log_weights, domain_ids, step_count):
    groups = lax.axis_size("x") * lax.axis_size("core")
    devices = lax.axis_size(FLAT)
    tok_rows = acts.shape[0]
    group_tok = devices // groups * tok_rows
    width = cotangent.shape[1]
    own_rows = weight.shape[0]
    core = lax.axis_index("core")
    shaped = acts.reshape(tok_rows, devices, own_rows)
    columns = lax.all_to_all(shaped, FLAT, split_axis=1, concat_axis=0, tiled=True)
    columns = columns.reshape(groups, group_tok, own_rows)
    mine = lax.all_gather(cotangent, ("x", "fsdp"), axis=0, tiled=True)
    mine = mine.reshape(groups // 2, group_tok, width)
    theirs = lax.ppermute(mine, "core", [(0, 1), (1, 0)])
    half = jnp.arange(groups // 2, dtype=jnp.int32) * 2
    order = jnp.concatenate([half + core, half + 1 - core])
    local_cols = jnp.take(columns, order, axis=0)
    dims = (((1,), (1,)), ((0,), (0,)))
    g_mine = lax.dot_general(local_cols[: groups // 2], mine, dims, preferred_element_type=jnp.float32)
    g_theirs = lax.dot_general(local_cols[groups // 2 :], theirs, dims, preferred_element_type=jnp.float32)
    owned = jnp.concatenate([g_mine, g_theirs]).astype(jnp.bfloat16)
    pairs = {}
    for i in range(groups):
        for j in range(i, groups):
            pairs[i, j] = jnp.sum(
                owned[i].astype(jnp.float32) * owned[j].astype(jnp.float32)
            )
    local_gram = jnp.stack(
        [jnp.stack([pairs[min(i, j), max(i, j)] for j in range(groups)]) for i in range(groups)]
    )
    perm = (order[:, None] == jnp.arange(groups, dtype=jnp.int32)[None, :]).astype(jnp.float32)
    device_gram = jnp.dot(
        perm.T, jnp.dot(local_gram, perm, precision=lax.Precision.HIGHEST),
        precision=lax.Precision.HIGHEST,
    )
    gram = lax.psum(device_gram, FLAT)
    score = jnp.sum(gram, axis=1) * (groups / jnp.trace(gram))
    onehot = (domain_ids[:, None] == jnp.arange(groups, dtype=jnp.int32)[None, :]).astype(
        jnp.float32
    )
    logits = log_weights + 2.0 * jnp.sum(onehot * score[:, None], axis=0)
    new_domain_weights = jax.nn.softmax(logits)
    group_w = jnp.sum(onehot * new_domain_weights[None, :], axis=1)
    local_w = jnp.take(group_w, order)
    combined = jnp.zeros((own_rows, width), jnp.float32)
    for group in range(groups):
        combined = combined + local_w[group] * owned[group].astype(jnp.float32)
    steps_f = step_count[0].astype(jnp.float32)
    new_moment = 0.9 * moment + 0.1 * combined
    new_second = 0.95 * second + 0.05 * combined * combined
    fix_one = 1.0 - jnp.exp(steps_f * jnp.log(jnp.float32(0.9)))
    fix_two = 1.0 - jnp.exp(steps_f * jnp.log(jnp.float32(0.95)))
    update = new_moment / fix_one / (jnp.sqrt(new_second / fix_two) + 1e-08)
    new_weight = (weight.astype(jnp.float32) - 0.002 * update).astype(jnp.bfloat16)
    return (new_weight, new_moment, new_second, new_domain_weights)


def solution(mesh):
    chips = mesh.shape["dom"] // 2
    flat = Mesh(mesh.devices.reshape(chips, 2, mesh.shape["fsdp"]), FLAT)
    row = P(FLAT, None)
    return jax.shard_map(
        on_device,
        mesh=flat,
        in_specs=(row, row, row, row, row, P(), P(), P()),
        out_specs=(row, row, row, P()),
        check_vma=False,
    )
```

```python
import jax
import jax.numpy as jnp
from jax import lax
from jax.sharding import Mesh, PartitionSpec as P

FLAT = ("x", "core", "fsdp")
SAME_CORE = ("x", "fsdp")


def on_device(acts, cotangent, weight, moment, second, log_weights, domain_ids, step_count):
    chips_x = lax.axis_size("x")
    members = lax.axis_size("fsdp")
    groups = chips_x * 2
    tok_rows = acts.shape[0]
    group_tok = members * tok_rows
    width = cotangent.shape[1]
    own_rows = weight.shape[0]
    core = lax.axis_index("core")
    shaped = acts.reshape(tok_rows, chips_x, 2, members, own_rows).transpose(0, 1, 3, 2, 4)
    shaped = shaped.reshape(tok_rows, chips_x * members, 2 * own_rows)
    columns = lax.all_to_all(shaped, SAME_CORE, split_axis=1, concat_axis=0, tiled=True)
    columns = columns.reshape(chips_x, group_tok, 2, own_rows)
    mine = lax.all_gather(cotangent, SAME_CORE, axis=0, tiled=True)
    mine = mine.reshape(chips_x, group_tok, width)
    dims = (((1,), (1,)), ((0,), (0,)))
    cols_partner = jnp.take(columns, 1 - core, axis=2)
    cols_own = jnp.take(columns, core, axis=2)
    g_partner = lax.dot_general(
        cols_partner, mine, dims, preferred_element_type=jnp.float32
    ).astype(jnp.bfloat16)
    received = lax.ppermute(g_partner, "core", [(0, 1), (1, 0)])
    g_own = lax.dot_general(
        cols_own, mine, dims, preferred_element_type=jnp.float32
    ).astype(jnp.bfloat16)
    owned = jnp.concatenate([g_own, received])
    half = jnp.arange(chips_x, dtype=jnp.int32) * 2
    order = jnp.concatenate([half + core, half + 1 - core])
    ids = jnp.arange(groups, dtype=jnp.int32)
    pos = jnp.where(ids % 2 == core, ids // 2, chips_x + ids // 2)
    pairs = {}
    for i in range(groups):
        for j in range(i, groups):
            pairs[i, j] = jnp.sum(
                owned[i].astype(jnp.float32) * owned[j].astype(jnp.float32)
            )
    local_gram = jnp.stack(
        [jnp.stack([pairs[min(i, j), max(i, j)] for j in range(groups)]) for i in range(groups)]
    )
    device_gram = jnp.take(jnp.take(local_gram, pos, axis=0), pos, axis=1)
    gram = lax.psum(lax.psum(lax.psum(device_gram, "core"), "x"), "fsdp")
    score = jnp.sum(gram, axis=1) * (groups / jnp.trace(gram))
    onehot = (domain_ids[:, None] == jnp.arange(groups, dtype=jnp.int32)[None, :]).astype(
        jnp.float32
    )
    logits = log_weights + 2.0 * jnp.sum(onehot * score[:, None], axis=0)
    new_domain_weights = jax.nn.softmax(logits)
    group_w = jnp.sum(onehot * new_domain_weights[None, :], axis=1)
    local_w = jnp.take(group_w, order)
    combined = jnp.zeros((own_rows, width), jnp.float32)
    for group in range(groups):
        combined = combined + local_w[group] * owned[group].astype(jnp.float32)
    steps_f = step_count[0].astype(jnp.float32)
    new_moment = 0.9 * moment + 0.1 * combined
    new_second = 0.95 * second + 0.05 * combined * combined
    fix_one = 1.0 - jnp.exp(steps_f * jnp.log(jnp.float32(0.9)))
    fix_two = 1.0 - jnp.exp(steps_f * jnp.log(jnp.float32(0.95)))
    update = new_moment / fix_one / (jnp.sqrt(new_second / fix_two) + 1e-08)
    new_weight = (weight.astype(jnp.float32) - 0.002 * update).astype(jnp.bfloat16)
    return (new_weight, new_moment, new_second, new_domain_weights)


def solution(mesh):
    chips = mesh.shape["dom"] // 2
    flat = Mesh(mesh.devices.reshape(chips, 2, mesh.shape["fsdp"]), FLAT)
    row = P(FLAT, None)
    return jax.shard_map(
        on_device,
        mesh=flat,
        in_specs=(row, row, row, row, row, P(), P(), P()),
        out_specs=(row, row, row, P()),
        check_vma=False,
    )
```

```python
import jax
import jax.numpy as jnp
from jax import lax
from jax.sharding import Mesh, PartitionSpec as P

FLAT = ("x", "core", "fsdp")
SAME_CORE = ("x", "fsdp")


def on_device(acts, cotangent, weight, moment, second, log_weights, domain_ids, step_count):
    chips_x = lax.axis_size("x")
    members = lax.axis_size("fsdp")
    groups = chips_x * 2
    tok_rows = acts.shape[0]
    group_tok = members * tok_rows
    width = cotangent.shape[1]
    own_rows = weight.shape[0]
    core = lax.axis_index("core")
    shaped = acts.reshape(tok_rows, chips_x, 2, members, own_rows).transpose(0, 1, 3, 2, 4)
    shaped = shaped.reshape(tok_rows, chips_x * members, 2 * own_rows)
    columns = lax.all_to_all(shaped, SAME_CORE, split_axis=1, concat_axis=0, tiled=True)
    columns = columns.reshape(chips_x, group_tok, 2, own_rows)
    mine = lax.all_gather(cotangent, SAME_CORE, axis=0, tiled=True)
    mine = mine.reshape(chips_x, group_tok, width)
    dims = (((1,), (1,)), ((0,), (0,)))
    cols_partner = jnp.take(columns, 1 - core, axis=2)
    cols_own = jnp.take(columns, core, axis=2)
    g_partner = lax.dot_general(
        cols_partner, mine, dims, preferred_element_type=jnp.float32
    ).astype(jnp.bfloat16)
    received = lax.ppermute(g_partner, "core", [(0, 1), (1, 0)])
    g_own = lax.dot_general(
        cols_own, mine, dims, preferred_element_type=jnp.float32
    ).astype(jnp.bfloat16)
    owned = jnp.concatenate([g_own, received])
    half = jnp.arange(chips_x, dtype=jnp.int32) * 2
    order = jnp.concatenate([half + core, half + 1 - core])
    pairs = {}
    for i in range(groups):
        for j in range(i, groups):
            pairs[i, j] = jnp.sum(
                owned[i].astype(jnp.float32) * owned[j].astype(jnp.float32)
            )
    ids_i = jnp.arange(groups, dtype=jnp.int32)[:, None]
    ids_j = jnp.arange(groups, dtype=jnp.int32)[None, :]
    device_gram = jnp.zeros((groups, groups), jnp.float32)
    for (i, j), value in pairs.items():
        gi, gj = order[i], order[j]
        hit = ((ids_i == gi) & (ids_j == gj)) | ((ids_i == gj) & (ids_j == gi))
        device_gram = device_gram + jnp.where(hit, value, 0.0)
    gram = lax.psum(lax.psum(lax.psum(device_gram, "core"), "x"), "fsdp")
    score = jnp.sum(gram, axis=1) * (groups / jnp.trace(gram))
    onehot = (domain_ids[:, None] == jnp.arange(groups, dtype=jnp.int32)[None, :]).astype(
        jnp.float32
    )
    logits = log_weights + 2.0 * jnp.sum(onehot * score[:, None], axis=0)
    new_domain_weights = jax.nn.softmax(logits)
    group_w = jnp.sum(onehot * new_domain_weights[None, :], axis=1)
    local_w = jnp.take(group_w, order)
    combined = jnp.zeros((own_rows, width), jnp.float32)
    for group in range(groups):
        combined = combined + local_w[group] * owned[group].astype(jnp.float32)
    steps_f = step_count[0].astype(jnp.float32)
    new_moment = 0.9 * moment + 0.1 * combined
    new_second = 0.95 * second + 0.05 * combined * combined
    fix_one = 1.0 - jnp.exp(steps_f * jnp.log(jnp.float32(0.9)))
    fix_two = 1.0 - jnp.exp(steps_f * jnp.log(jnp.float32(0.95)))
    update = new_moment / fix_one / (jnp.sqrt(new_second / fix_two) + 1e-08)
    new_weight = (weight.astype(jnp.float32) - 0.002 * update).astype(jnp.bfloat16)
    return (new_weight, new_moment, new_second, new_domain_weights)


def solution(mesh):
    chips = mesh.shape["dom"] // 2
    flat = Mesh(mesh.devices.reshape(chips, 2, mesh.shape["fsdp"]), FLAT)
    row = P(FLAT, None)
    return jax.shard_map(
        on_device,
        mesh=flat,
        in_specs=(row, row, row, row, row, P(), P(), P()),
        out_specs=(row, row, row, P()),
        check_vma=False,
    )
```

```python
import jax
import jax.numpy as jnp
from jax import lax
from jax.sharding import Mesh, PartitionSpec as P

FLAT = ("x", "core", "fsdp", "pair")
SAME_CORE = ("x", "fsdp", "pair")


def on_device(acts, cotangent, weight, moment, second, log_weights, domain_ids, step_count):
    chips_x = lax.axis_size("x")
    members = lax.axis_size("fsdp") * lax.axis_size("pair")
    groups = chips_x * 2
    tok_rows = acts.shape[0]
    group_tok = members * tok_rows
    width = cotangent.shape[1]
    own_rows = weight.shape[0]
    core = lax.axis_index("core")
    shaped = acts.reshape(tok_rows, chips_x, 2, members, own_rows).transpose(0, 1, 3, 2, 4)
    shaped = shaped.reshape(tok_rows, chips_x * members, 2 * own_rows)
    columns = lax.all_to_all(shaped, SAME_CORE, split_axis=1, concat_axis=0, tiled=True)
    columns = columns.reshape(chips_x, group_tok, 2, own_rows)
    mine = lax.all_gather(cotangent, SAME_CORE, axis=0, tiled=True)
    mine = mine.reshape(chips_x, group_tok, width)
    dims = (((1,), (1,)), ((0,), (0,)))
    cols_partner = jnp.take(columns, 1 - core, axis=2)
    cols_own = jnp.take(columns, core, axis=2)
    g_partner = lax.dot_general(
        cols_partner, mine, dims, preferred_element_type=jnp.float32
    ).astype(jnp.bfloat16)
    received = lax.ppermute(g_partner, "core", [(0, 1), (1, 0)])
    g_own = lax.dot_general(
        cols_own, mine, dims, preferred_element_type=jnp.float32
    ).astype(jnp.bfloat16)
    owned = jnp.concatenate([g_own, received])
    half = jnp.arange(chips_x, dtype=jnp.int32) * 2
    order = jnp.concatenate([half + core, half + 1 - core])
    keys = [(i, j) for i in range(groups) for j in range(i, groups)]
    partial = jnp.stack(
        [
            jnp.sum(owned[i].astype(jnp.float32) * owned[j].astype(jnp.float32), axis=0)
            for i, j in keys
        ]
    )
    sums = jnp.sum(partial, axis=1)
    ids_i = jnp.arange(groups, dtype=jnp.int32)[:, None]
    ids_j = jnp.arange(groups, dtype=jnp.int32)[None, :]
    device_gram = jnp.zeros((groups, groups), jnp.float32)
    for n, (i, j) in enumerate(keys):
        gi, gj = order[i], order[j]
        hit = ((ids_i == gi) & (ids_j == gj)) | ((ids_i == gj) & (ids_j == gi))
        device_gram = device_gram + jnp.where(hit, sums[n], 0.0)
    gram = device_gram
    for axis in ("core", "pair", "x", "fsdp"):
        gram = lax.psum(gram, axis)
    score = jnp.sum(gram, axis=1) * (groups / jnp.trace(gram))
    onehot = (domain_ids[:, None] == jnp.arange(groups, dtype=jnp.int32)[None, :]).astype(
        jnp.float32
    )
    logits = log_weights + 2.0 * jnp.sum(onehot * score[:, None], axis=0)
    new_domain_weights = jax.nn.softmax(logits)
    group_w = jnp.sum(onehot * new_domain_weights[None, :], axis=1)
    local_w = jnp.take(group_w, order)
    combined = jnp.zeros((own_rows, width), jnp.float32)
    for group in range(groups):
        combined = combined + local_w[group] * owned[group].astype(jnp.float32)
    steps_f = step_count[0].astype(jnp.float32)
    new_moment = 0.9 * moment + 0.1 * combined
    new_second = 0.95 * second + 0.05 * combined * combined
    fix_one = 1.0 - jnp.exp(steps_f * jnp.log(jnp.float32(0.9)))
    fix_two = 1.0 - jnp.exp(steps_f * jnp.log(jnp.float32(0.95)))
    update = new_moment / fix_one / (jnp.sqrt(new_second / fix_two) + 1e-08)
    new_weight = (weight.astype(jnp.float32) - 0.002 * update).astype(jnp.bfloat16)
    return (new_weight, new_moment, new_second, new_domain_weights)


def solution(mesh):
    chips = mesh.shape["dom"] // 2
    flat = Mesh(mesh.devices.reshape(chips, 2, mesh.shape["fsdp"] // 2, 2), FLAT)
    row = P(FLAT, None)
    return jax.shard_map(
        on_device,
        mesh=flat,
        in_specs=(row, row, row, row, row, P(), P(), P()),
        out_specs=(row, row, row, P()),
        check_vma=False,
    )
```

```python
import jax
import jax.numpy as jnp
from jax import lax
from jax.sharding import Mesh, PartitionSpec as P

FLAT = ("x", "core", "fsdp", "pair")
SAME_CORE = ("x", "fsdp", "pair")


def on_device(acts, cotangent, weight, moment, second, log_weights, domain_ids, step_count):
    chips_x = lax.axis_size("x")
    members = lax.axis_size("fsdp") * lax.axis_size("pair")
    groups = chips_x * 2
    tok_rows = acts.shape[0]
    group_tok = members * tok_rows
    width = cotangent.shape[1]
    own_rows = weight.shape[0]
    core = lax.axis_index("core")
    shaped = acts.reshape(tok_rows, chips_x, 2, members, own_rows).transpose(0, 1, 3, 2, 4)
    shaped = shaped.reshape(tok_rows, chips_x * members, 2 * own_rows)
    columns = lax.all_to_all(shaped, SAME_CORE, split_axis=1, concat_axis=0, tiled=True)
    columns = columns.reshape(chips_x, group_tok, 2, own_rows)
    mine = lax.all_gather(cotangent, SAME_CORE, axis=0, tiled=True)
    mine = mine.reshape(chips_x, group_tok, width)
    dims = (((1,), (1,)), ((0,), (0,)))
    cols_partner = jnp.take(columns, 1 - core, axis=2)
    cols_own = jnp.take(columns, core, axis=2)
    g_partner = lax.dot_general(
        cols_partner, mine, dims, preferred_element_type=jnp.float32
    ).astype(jnp.bfloat16)
    received = lax.ppermute(g_partner, "core", [(0, 1), (1, 0)])
    g_own = lax.dot_general(
        cols_own, mine, dims, preferred_element_type=jnp.float32
    ).astype(jnp.bfloat16)
    owned = jnp.concatenate([g_own, received])
    half = jnp.arange(chips_x, dtype=jnp.int32) * 2
    order = jnp.concatenate([half + core, half + 1 - core])
    keys = [(i, j) for i in range(groups) for j in range(i, groups)]
    partial = jnp.stack(
        [
            jnp.sum(owned[i].astype(jnp.float32) * owned[j].astype(jnp.float32), axis=0)
            for i, j in keys
        ]
    )
    sums = jnp.sum(partial, axis=1)
    ids = jnp.arange(groups, dtype=jnp.int32)
    pos = jnp.where(ids % 2 == core, ids // 2, chips_x + ids // 2)
    lo = jnp.minimum(pos[:, None], pos[None, :])
    hi = jnp.maximum(pos[:, None], pos[None, :])
    device_gram = jnp.take(sums, lo * groups - lo * (lo - 1) // 2 + (hi - lo))
    gram = device_gram
    for axis in ("core", "pair", "x", "fsdp"):
        gram = lax.psum(gram, axis)
    score = jnp.sum(gram, axis=1) * (groups / jnp.trace(gram))
    onehot = (domain_ids[:, None] == jnp.arange(groups, dtype=jnp.int32)[None, :]).astype(
        jnp.float32
    )
    logits = log_weights + 2.0 * jnp.sum(onehot * score[:, None], axis=0)
    new_domain_weights = jax.nn.softmax(logits)
    group_w = jnp.sum(onehot * new_domain_weights[None, :], axis=1)
    local_w = jnp.take(group_w, order)
    combined = jnp.zeros((own_rows, width), jnp.float32)
    for group in range(groups):
        combined = combined + local_w[group] * owned[group].astype(jnp.float32)
    steps_f = step_count[0].astype(jnp.float32)
    new_moment = 0.9 * moment + 0.1 * combined
    new_second = 0.95 * second + 0.05 * combined * combined
    fix_one = 1.0 - jnp.exp(steps_f * jnp.log(jnp.float32(0.9)))
    fix_two = 1.0 - jnp.exp(steps_f * jnp.log(jnp.float32(0.95)))
    update = new_moment / fix_one / (jnp.sqrt(new_second / fix_two) + 1e-08)
    new_weight = (weight.astype(jnp.float32) - 0.002 * update).astype(jnp.bfloat16)
    return (new_weight, new_moment, new_second, new_domain_weights)


def solution(mesh):
    chips = mesh.shape["dom"] // 2
    flat = Mesh(mesh.devices.reshape(chips, 2, mesh.shape["fsdp"] // 2, 2), FLAT)
    row = P(FLAT, None)
    return jax.shard_map(
        on_device,
        mesh=flat,
        in_specs=(row, row, row, row, row, P(), P(), P()),
        out_specs=(row, row, row, P()),
        check_vma=False,
    )
```

```python
import jax
import jax.numpy as jnp
from jax import lax
from jax.sharding import Mesh, PartitionSpec as P

FLAT = ("x", "core", "fsdp", "pair")
SAME_CORE = ("x", "fsdp", "pair")


def on_device(acts, cotangent, weight, moment, second, log_weights, domain_ids, step_count):
    chips_x = lax.axis_size("x")
    members = lax.axis_size("fsdp") * lax.axis_size("pair")
    groups = chips_x * 2
    tok_rows = acts.shape[0]
    group_tok = members * tok_rows
    width = cotangent.shape[1]
    own_rows = weight.shape[0]
    core = lax.axis_index("core")
    shaped = acts.reshape(tok_rows, chips_x, 2, members, own_rows).transpose(0, 1, 3, 2, 4)
    shaped = shaped.reshape(tok_rows, chips_x * members, 2 * own_rows)
    columns = lax.all_to_all(shaped, SAME_CORE, split_axis=1, concat_axis=0, tiled=True)
    columns = columns.reshape(chips_x, group_tok, 2, own_rows)
    mine = lax.all_gather(cotangent, SAME_CORE, axis=0, tiled=True)
    mine = mine.reshape(chips_x, group_tok, width)
    dims = (((1,), (1,)), ((0,), (0,)))
    cols_partner = jnp.take(columns, 1 - core, axis=2)
    cols_own = jnp.take(columns, core, axis=2)
    g_partner = lax.dot_general(
        cols_partner, mine, dims, preferred_element_type=jnp.float32
    ).astype(jnp.bfloat16)
    received = lax.ppermute(g_partner, "core", [(0, 1), (1, 0)])
    g_own = lax.dot_general(
        cols_own, mine, dims, preferred_element_type=jnp.float32
    ).astype(jnp.bfloat16)
    owned = jnp.concatenate([g_own, received])
    half = jnp.arange(chips_x, dtype=jnp.int32) * 2
    order = jnp.concatenate([half + core, half + 1 - core])
    keys = [(i, j) for i in range(groups) for j in range(i, groups)]
    partial = jnp.stack(
        [
            jnp.sum(owned[i].astype(jnp.float32) * owned[j].astype(jnp.float32), axis=0)
            for i, j in keys
        ]
    )
    sums = jnp.sum(partial, axis=1)
    ids = jnp.arange(groups, dtype=jnp.int32)
    pos = jnp.where(ids % 2 == core, ids // 2, chips_x + ids // 2)
    lo = jnp.minimum(pos[:, None], pos[None, :])
    hi = jnp.maximum(pos[:, None], pos[None, :])
    device_gram = jnp.take(sums, lo * groups - lo * (lo - 1) // 2 + (hi - lo))
    gram = device_gram
    for axes in (("core",), ("pair", "x"), ("fsdp",)):
        gram = lax.psum(gram, axes)
    score = jnp.sum(gram, axis=1) * (groups / jnp.trace(gram))
    onehot = (domain_ids[:, None] == jnp.arange(groups, dtype=jnp.int32)[None, :]).astype(
        jnp.float32
    )
    logits = log_weights + 2.0 * jnp.sum(onehot * score[:, None], axis=0)
    new_domain_weights = jax.nn.softmax(logits)
    group_w = jnp.sum(onehot * new_domain_weights[None, :], axis=1)
    local_w = jnp.take(group_w, order)
    combined = jnp.zeros((own_rows, width), jnp.float32)
    for group in range(groups):
        combined = combined + local_w[group] * owned[group].astype(jnp.float32)
    steps_f = step_count[0].astype(jnp.float32)
    new_moment = 0.9 * moment + 0.1 * combined
    new_second = 0.95 * second + 0.05 * combined * combined
    fix_one = 1.0 - jnp.exp(steps_f * jnp.log(jnp.float32(0.9)))
    fix_two = 1.0 - jnp.exp(steps_f * jnp.log(jnp.float32(0.95)))
    update = new_moment / fix_one / (jnp.sqrt(new_second / fix_two) + 1e-08)
    new_weight = (weight.astype(jnp.float32) - 0.002 * update).astype(jnp.bfloat16)
    return (new_weight, new_moment, new_second, new_domain_weights)


def solution(mesh):
    chips = mesh.shape["dom"] // 2
    flat = Mesh(mesh.devices.reshape(chips, 2, mesh.shape["fsdp"] // 2, 2), FLAT)
    row = P(FLAT, None)
    return jax.shard_map(
        on_device,
        mesh=flat,
        in_specs=(row, row, row, row, row, P(), P(), P()),
        out_specs=(row, row, row, P()),
        check_vma=False,
    )
```

```python
import jax
import jax.numpy as jnp
from jax import lax
from jax.experimental import pallas as pl
from jax.experimental.pallas import tpu as pltpu
from jax.sharding import Mesh, PartitionSpec as P

FLAT = ("x", "core", "fsdp", "pair")
SAME_CORE = ("x", "fsdp", "pair")


def adam_kernel(scal_ref, own_ref, recv_ref, m_ref, s_ref, w_ref, nw_ref, nm_ref, ns_ref):
    half = own_ref.shape[0]
    combined = scal_ref[0] * own_ref[0].astype(jnp.float32)
    for k in range(1, half):
        combined = combined + scal_ref[k] * own_ref[k].astype(jnp.float32)
    for k in range(half):
        combined = combined + scal_ref[half + k] * recv_ref[k].astype(jnp.float32)
    fix_one = scal_ref[2 * half]
    fix_two = scal_ref[2 * half + 1]
    new_moment = 0.9 * m_ref[...] + 0.1 * combined
    new_second = 0.95 * s_ref[...] + 0.05 * combined * combined
    update = new_moment / fix_one / (jnp.sqrt(new_second / fix_two) + 1e-08)
    nw_ref[...] = (w_ref[...].astype(jnp.float32) - 0.002 * update).astype(nw_ref.dtype)
    nm_ref[...] = new_moment
    ns_ref[...] = new_second


def adam_update(scal, g_own, received, moment, second, weight):
    half, rows, width = g_own.shape
    tile = next(t for t in (64, 32, 16, rows) if rows % t == 0)
    grad_spec = pl.BlockSpec((half, tile, width), lambda i: (0, i, 0))
    row_spec = pl.BlockSpec((tile, width), lambda i: (i, 0))
    elems = rows * width
    return pl.pallas_call(
        adam_kernel,
        grid=(rows // tile,),
        in_specs=[
            pl.BlockSpec(memory_space=pltpu.SMEM),
            grad_spec,
            grad_spec,
            row_spec,
            row_spec,
            row_spec,
        ],
        out_specs=[row_spec, row_spec, row_spec],
        out_shape=[
            jax.ShapeDtypeStruct((rows, width), weight.dtype),
            jax.ShapeDtypeStruct((rows, width), jnp.float32),
            jax.ShapeDtypeStruct((rows, width), jnp.float32),
        ],
        cost_estimate=pl.CostEstimate(
            flops=20 * elems, transcendentals=2 * elems, bytes_accessed=elems * (4 * half + 20)
        ),
    )(scal, g_own, received, moment, second, weight)


def on_device(acts, cotangent, weight, moment, second, log_weights, domain_ids, step_count):
    chips_x = lax.axis_size("x")
    members = lax.axis_size("fsdp") * lax.axis_size("pair")
    groups = chips_x * 2
    tok_rows = acts.shape[0]
    group_tok = members * tok_rows
    width = cotangent.shape[1]
    own_rows = weight.shape[0]
    core = lax.axis_index("core")
    shaped = acts.reshape(tok_rows, chips_x, 2, members, own_rows).transpose(0, 1, 3, 2, 4)
    shaped = shaped.reshape(tok_rows, chips_x * members, 2 * own_rows)
    columns = lax.all_to_all(shaped, SAME_CORE, split_axis=1, concat_axis=0, tiled=True)
    columns = columns.reshape(chips_x, group_tok, 2, own_rows)
    mine = lax.all_gather(cotangent, SAME_CORE, axis=0, tiled=True)
    mine = mine.reshape(chips_x, group_tok, width)
    dims = (((1,), (1,)), ((0,), (0,)))
    cols_partner = jnp.take(columns, 1 - core, axis=2)
    cols_own = jnp.take(columns, core, axis=2)
    g_partner = lax.dot_general(
        cols_partner, mine, dims, preferred_element_type=jnp.float32
    ).astype(jnp.bfloat16)
    received = lax.ppermute(g_partner, "core", [(0, 1), (1, 0)])
    g_own = lax.dot_general(
        cols_own, mine, dims, preferred_element_type=jnp.float32
    ).astype(jnp.bfloat16)
    owned = jnp.concatenate([g_own, received])
    half = jnp.arange(chips_x, dtype=jnp.int32) * 2
    order = jnp.concatenate([half + core, half + 1 - core])
    keys = [(i, j) for i in range(groups) for j in range(i, groups)]
    partial = jnp.stack(
        [
            jnp.sum(owned[i].astype(jnp.float32) * owned[j].astype(jnp.float32), axis=0)
            for i, j in keys
        ]
    )
    sums = jnp.sum(partial, axis=1)
    ids = jnp.arange(groups, dtype=jnp.int32)
    pos = jnp.where(ids % 2 == core, ids // 2, chips_x + ids // 2)
    lo = jnp.minimum(pos[:, None], pos[None, :])
    hi = jnp.maximum(pos[:, None], pos[None, :])
    device_gram = jnp.take(sums, lo * groups - lo * (lo - 1) // 2 + (hi - lo))
    gram = device_gram
    for axes in (("core",), ("pair", "x"), ("fsdp",)):
        gram = lax.psum(gram, axes)
    score = jnp.sum(gram, axis=1) * (groups / jnp.trace(gram))
    onehot = (domain_ids[:, None] == jnp.arange(groups, dtype=jnp.int32)[None, :]).astype(
        jnp.float32
    )
    logits = log_weights + 2.0 * jnp.sum(onehot * score[:, None], axis=0)
    new_domain_weights = jax.nn.softmax(logits)
    group_w = jnp.sum(onehot * new_domain_weights[None, :], axis=1)
    local_w = jnp.take(group_w, order)
    steps_f = step_count[0].astype(jnp.float32)
    fix_one = 1.0 - jnp.exp(steps_f * jnp.log(jnp.float32(0.9)))
    fix_two = 1.0 - jnp.exp(steps_f * jnp.log(jnp.float32(0.95)))
    scal = jnp.concatenate([local_w, jnp.stack([fix_one, fix_two])])
    new_weight, new_moment, new_second = adam_update(scal, g_own, received, moment, second, weight)
    return (new_weight, new_moment, new_second, new_domain_weights)


def solution(mesh):
    chips = mesh.shape["dom"] // 2
    flat = Mesh(mesh.devices.reshape(chips, 2, mesh.shape["fsdp"] // 2, 2), FLAT)
    row = P(FLAT, None)
    return jax.shard_map(
        on_device,
        mesh=flat,
        in_specs=(row, row, row, row, row, P(), P(), P()),
        out_specs=(row, row, row, P()),
        check_vma=False,
    )
```

```python
import jax
import jax.numpy as jnp
from jax import lax
from jax.experimental import pallas as pl
from jax.experimental.pallas import tpu as pltpu
from jax.sharding import Mesh, PartitionSpec as P

FLAT = ("x", "core", "fsdp", "pair")
SAME_CORE = ("x", "fsdp", "pair")


def adam_kernel(scal_ref, own_ref, recv_ref, m_ref, s_ref, w_ref, nw_ref, nm_ref, ns_ref):
    half = own_ref.shape[0]
    combined = scal_ref[0] * own_ref[0].astype(jnp.float32)
    for k in range(1, half):
        combined = combined + scal_ref[k] * own_ref[k].astype(jnp.float32)
    for k in range(half):
        combined = combined + scal_ref[half + k] * recv_ref[k].astype(jnp.float32)
    fix_one = scal_ref[2 * half]
    fix_two = scal_ref[2 * half + 1]
    new_moment = 0.9 * m_ref[...] + 0.1 * combined
    new_second = 0.95 * s_ref[...] + 0.05 * combined * combined
    update = new_moment / fix_one / (jnp.sqrt(new_second / fix_two) + 1e-08)
    nw_ref[...] = (w_ref[...].astype(jnp.float32) - 0.002 * update).astype(nw_ref.dtype)
    nm_ref[...] = new_moment
    ns_ref[...] = new_second


def adam_update(scal, g_own, received, moment, second, weight):
    half, rows, width = g_own.shape
    tile = next(t for t in (112, 64, 32, 16, rows) if rows % t == 0)
    grad_spec = pl.BlockSpec((half, tile, width), lambda i: (0, i, 0))
    row_spec = pl.BlockSpec((tile, width), lambda i: (i, 0))
    elems = rows * width
    return pl.pallas_call(
        adam_kernel,
        grid=(rows // tile,),
        in_specs=[
            pl.BlockSpec(memory_space=pltpu.SMEM),
            grad_spec,
            grad_spec,
            row_spec,
            row_spec,
            row_spec,
        ],
        out_specs=[row_spec, row_spec, row_spec],
        out_shape=[
            jax.ShapeDtypeStruct((rows, width), weight.dtype),
            jax.ShapeDtypeStruct((rows, width), jnp.float32),
            jax.ShapeDtypeStruct((rows, width), jnp.float32),
        ],
        cost_estimate=pl.CostEstimate(
            flops=20 * elems, transcendentals=2 * elems, bytes_accessed=elems * (4 * half + 20)
        ),
    )(scal, g_own, received, moment, second, weight)


def on_device(acts, cotangent, weight, moment, second, log_weights, domain_ids, step_count):
    chips_x = lax.axis_size("x")
    members = lax.axis_size("fsdp") * lax.axis_size("pair")
    groups = chips_x * 2
    tok_rows = acts.shape[0]
    group_tok = members * tok_rows
    width = cotangent.shape[1]
    own_rows = weight.shape[0]
    core = lax.axis_index("core")
    shaped = acts.reshape(tok_rows, chips_x, 2, members, own_rows).transpose(0, 1, 3, 2, 4)
    shaped = shaped.reshape(tok_rows, chips_x * members, 2 * own_rows)
    columns = lax.all_to_all(shaped, SAME_CORE, split_axis=1, concat_axis=0, tiled=True)
    columns = columns.reshape(chips_x, group_tok, 2, own_rows)
    mine = lax.all_gather(cotangent, SAME_CORE, axis=0, tiled=True)
    mine = mine.reshape(chips_x, group_tok, width)
    dims = (((1,), (1,)), ((0,), (0,)))
    cols_partner = jnp.take(columns, 1 - core, axis=2)
    cols_own = jnp.take(columns, core, axis=2)
    g_partner = lax.dot_general(
        cols_partner, mine, dims, preferred_element_type=jnp.float32
    ).astype(jnp.bfloat16)
    received = lax.ppermute(g_partner, "core", [(0, 1), (1, 0)])
    g_own = lax.dot_general(
        cols_own, mine, dims, preferred_element_type=jnp.float32
    ).astype(jnp.bfloat16)
    owned = jnp.concatenate([g_own, received])
    half = jnp.arange(chips_x, dtype=jnp.int32) * 2
    order = jnp.concatenate([half + core, half + 1 - core])
    keys = [(i, j) for i in range(groups) for j in range(i, groups)]
    partial = jnp.stack(
        [
            jnp.sum(owned[i].astype(jnp.float32) * owned[j].astype(jnp.float32), axis=0)
            for i, j in keys
        ]
    )
    sums = jnp.sum(partial, axis=1)
    ids = jnp.arange(groups, dtype=jnp.int32)
    pos = jnp.where(ids % 2 == core, ids // 2, chips_x + ids // 2)
    lo = jnp.minimum(pos[:, None], pos[None, :])
    hi = jnp.maximum(pos[:, None], pos[None, :])
    device_gram = jnp.take(sums, lo * groups - lo * (lo - 1) // 2 + (hi - lo))
    gram = device_gram
    for axes in (("core",), ("pair", "x"), ("fsdp",)):
        gram = lax.psum(gram, axes)
    score = jnp.sum(gram, axis=1) * (groups / jnp.trace(gram))
    onehot = (domain_ids[:, None] == jnp.arange(groups, dtype=jnp.int32)[None, :]).astype(
        jnp.float32
    )
    logits = log_weights + 2.0 * jnp.sum(onehot * score[:, None], axis=0)
    new_domain_weights = jax.nn.softmax(logits)
    group_w = jnp.sum(onehot * new_domain_weights[None, :], axis=1)
    local_w = jnp.take(group_w, order)
    steps_f = step_count[0].astype(jnp.float32)
    fix_one = 1.0 - jnp.exp(steps_f * jnp.log(jnp.float32(0.9)))
    fix_two = 1.0 - jnp.exp(steps_f * jnp.log(jnp.float32(0.95)))
    scal = jnp.concatenate([local_w, jnp.stack([fix_one, fix_two])])
    new_weight, new_moment, new_second = adam_update(scal, g_own, received, moment, second, weight)
    return (new_weight, new_moment, new_second, new_domain_weights)


def solution(mesh):
    chips = mesh.shape["dom"] // 2
    flat = Mesh(mesh.devices.reshape(chips, 2, mesh.shape["fsdp"] // 2, 2), FLAT)
    row = P(FLAT, None)
    return jax.shard_map(
        on_device,
        mesh=flat,
        in_specs=(row, row, row, row, row, P(), P(), P()),
        out_specs=(row, row, row, P()),
        check_vma=False,
    )
```

```python
import jax
import jax.numpy as jnp
from jax import lax
from jax.experimental import pallas as pl
from jax.experimental.pallas import tpu as pltpu
from jax.sharding import Mesh, PartitionSpec as P

FLAT = ("x", "core", "fsdp", "pair")
SAME_CORE = ("x", "fsdp", "pair")


def adam_kernel(scal_ref, own_ref, recv_ref, m_ref, s_ref, w_ref, nw_ref, nm_ref, ns_ref):
    half = own_ref.shape[0]
    combined = scal_ref[0] * own_ref[0].astype(jnp.float32)
    for k in range(1, half):
        combined = combined + scal_ref[k] * own_ref[k].astype(jnp.float32)
    for k in range(half):
        combined = combined + scal_ref[half + k] * recv_ref[k].astype(jnp.float32)
    fix_one = scal_ref[2 * half]
    fix_two = scal_ref[2 * half + 1]
    new_moment = 0.9 * m_ref[...] + 0.1 * combined
    new_second = 0.95 * s_ref[...] + 0.05 * combined * combined
    update = new_moment / fix_one / (jnp.sqrt(new_second / fix_two) + 1e-08)
    nw_ref[...] = (w_ref[...].astype(jnp.float32) - 0.002 * update).astype(nw_ref.dtype)
    nm_ref[...] = new_moment
    ns_ref[...] = new_second


def adam_update(scal, g_own, received, moment, second, weight):
    half, rows, width = g_own.shape
    tile = next(t for t in (112, 64, 32, 16, rows) if rows % t == 0)
    grad_spec = pl.BlockSpec((half, tile, width), lambda i: (0, i, 0))
    row_spec = pl.BlockSpec((tile, width), lambda i: (i, 0))
    elems = rows * width
    return pl.pallas_call(
        adam_kernel,
        grid=(rows // tile,),
        in_specs=[
            pl.BlockSpec(memory_space=pltpu.SMEM),
            grad_spec,
            grad_spec,
            row_spec,
            row_spec,
            row_spec,
        ],
        out_specs=[row_spec, row_spec, row_spec],
        out_shape=[
            jax.ShapeDtypeStruct((rows, width), weight.dtype),
            jax.ShapeDtypeStruct((rows, width), jnp.float32),
            jax.ShapeDtypeStruct((rows, width), jnp.float32),
        ],
        cost_estimate=pl.CostEstimate(
            flops=20 * elems, transcendentals=2 * elems, bytes_accessed=elems * (4 * half + 20)
        ),
    )(scal, g_own, received, moment, second, weight)


def on_device(acts, cotangent, weight, moment, second, log_weights, domain_ids, step_count):
    chips_x = lax.axis_size("x")
    members = lax.axis_size("fsdp") * lax.axis_size("pair")
    groups = chips_x * 2
    tok_rows = acts.shape[0]
    group_tok = members * tok_rows
    width = cotangent.shape[1]
    own_rows = weight.shape[0]
    core = lax.axis_index("core")
    shaped = acts.reshape(tok_rows, chips_x, 2, members, own_rows).transpose(0, 1, 3, 2, 4)
    shaped = shaped.reshape(tok_rows, chips_x * members, 2 * own_rows)
    columns = lax.all_to_all(shaped, SAME_CORE, split_axis=1, concat_axis=0, tiled=True)
    columns = columns.reshape(chips_x, group_tok, 2, own_rows)
    mine = lax.all_gather(cotangent, SAME_CORE, axis=0, tiled=True)
    mine = mine.reshape(chips_x, group_tok, width)
    dims = (((1,), (1,)), ((0,), (0,)))
    cols_partner = jnp.take(columns, 1 - core, axis=2)
    cols_own = jnp.take(columns, core, axis=2)
    g_partner = lax.dot_general(
        cols_partner, mine, dims, preferred_element_type=jnp.float32
    ).astype(jnp.bfloat16)
    received = lax.ppermute(g_partner, "core", [(0, 1), (1, 0)])
    g_own = lax.dot_general(
        cols_own, mine, dims, preferred_element_type=jnp.float32
    ).astype(jnp.bfloat16)
    owned = jnp.concatenate([g_own, received])
    half = jnp.arange(chips_x, dtype=jnp.int32) * 2
    order = jnp.concatenate([half + core, half + 1 - core])
    keys = [(i, j) for i in range(groups) for j in range(i, groups)]
    partial = jnp.stack(
        [
            jnp.sum(owned[i].astype(jnp.float32) * owned[j].astype(jnp.float32), axis=0)
            for i, j in keys
        ]
    )
    sums = jnp.sum(partial, axis=1)
    ids = jnp.arange(groups, dtype=jnp.int32)
    pos = jnp.where(ids % 2 == core, ids // 2, chips_x + ids // 2)
    lo = jnp.minimum(pos[:, None], pos[None, :])
    hi = jnp.maximum(pos[:, None], pos[None, :])
    device_gram = jnp.take(sums, lo * groups - lo * (lo - 1) // 2 + (hi - lo))
    gram = device_gram
    for axes in (("core", "pair", "x"), ("fsdp",)):
        gram = lax.psum(gram, axes)
    score = jnp.sum(gram, axis=1) * (groups / jnp.trace(gram))
    onehot = (domain_ids[:, None] == jnp.arange(groups, dtype=jnp.int32)[None, :]).astype(
        jnp.float32
    )
    logits = log_weights + 2.0 * jnp.sum(onehot * score[:, None], axis=0)
    new_domain_weights = jax.nn.softmax(logits)
    group_w = jnp.sum(onehot * new_domain_weights[None, :], axis=1)
    local_w = jnp.take(group_w, order)
    steps_f = step_count[0].astype(jnp.float32)
    fix_one = 1.0 - jnp.exp(steps_f * jnp.log(jnp.float32(0.9)))
    fix_two = 1.0 - jnp.exp(steps_f * jnp.log(jnp.float32(0.95)))
    scal = jnp.concatenate([local_w, jnp.stack([fix_one, fix_two])])
    new_weight, new_moment, new_second = adam_update(scal, g_own, received, moment, second, weight)
    return (new_weight, new_moment, new_second, new_domain_weights)


def solution(mesh):
    chips = mesh.shape["dom"] // 2
    flat = Mesh(mesh.devices.reshape(chips, 2, mesh.shape["fsdp"] // 2, 2), FLAT)
    row = P(FLAT, None)
    return jax.shard_map(
        on_device,
        mesh=flat,
        in_specs=(row, row, row, row, row, P(), P(), P()),
        out_specs=(row, row, row, P()),
        check_vma=False,
    )
```

```python
import jax
import jax.numpy as jnp
from jax import lax
from jax.experimental import pallas as pl
from jax.experimental.pallas import tpu as pltpu
from jax.sharding import Mesh, PartitionSpec as P

FLAT = ("x", "core", "fsdp", "pair")
SAME_CORE = ("x", "fsdp", "pair")


def adam_kernel(scal_ref, own_ref, recv_ref, m_ref, s_ref, w_ref, nw_ref, nm_ref, ns_ref):
    half = own_ref.shape[0]
    combined = scal_ref[0] * own_ref[0].astype(jnp.float32)
    for k in range(1, half):
        combined = combined + scal_ref[k] * own_ref[k].astype(jnp.float32)
    for k in range(half):
        combined = combined + scal_ref[half + k] * recv_ref[k].astype(jnp.float32)
    fix_one = scal_ref[2 * half]
    fix_two = scal_ref[2 * half + 1]
    new_moment = 0.9 * m_ref[...] + 0.1 * combined
    new_second = 0.95 * s_ref[...] + 0.05 * combined * combined
    update = new_moment / fix_one / (jnp.sqrt(new_second / fix_two) + 1e-08)
    nw_ref[...] = (w_ref[...].astype(jnp.float32) - 0.002 * update).astype(nw_ref.dtype)
    nm_ref[...] = new_moment
    ns_ref[...] = new_second


def adam_update(scal, g_own, received, moment, second, weight):
    half, rows, width = g_own.shape
    tile = next(t for t in (112, 64, 32, 16, rows) if rows % t == 0)
    grad_spec = pl.BlockSpec((half, tile, width), lambda i: (0, i, 0))
    row_spec = pl.BlockSpec((tile, width), lambda i: (i, 0))
    elems = rows * width
    return pl.pallas_call(
        adam_kernel,
        grid=(rows // tile,),
        in_specs=[
            pl.BlockSpec(memory_space=pltpu.SMEM),
            grad_spec,
            grad_spec,
            row_spec,
            row_spec,
            row_spec,
        ],
        out_specs=[row_spec, row_spec, row_spec],
        out_shape=[
            jax.ShapeDtypeStruct((rows, width), weight.dtype),
            jax.ShapeDtypeStruct((rows, width), jnp.float32),
            jax.ShapeDtypeStruct((rows, width), jnp.float32),
        ],
        cost_estimate=pl.CostEstimate(
            flops=20 * elems, transcendentals=2 * elems, bytes_accessed=elems * (4 * half + 20)
        ),
    )(scal, g_own, received, moment, second, weight)


def on_device(acts, cotangent, weight, moment, second, log_weights, domain_ids, step_count):
    chips_x = lax.axis_size("x")
    members = lax.axis_size("fsdp") * lax.axis_size("pair")
    groups = chips_x * 2
    tok_rows = acts.shape[0]
    group_tok = members * tok_rows
    width = cotangent.shape[1]
    own_rows = weight.shape[0]
    core = lax.axis_index("core")
    shaped = acts.reshape(tok_rows, chips_x, 2, members, own_rows).transpose(0, 1, 3, 2, 4)
    shaped = shaped.reshape(tok_rows, chips_x * members, 2 * own_rows)
    columns = lax.all_to_all(shaped, SAME_CORE, split_axis=1, concat_axis=0, tiled=True)
    columns = columns.reshape(chips_x, group_tok, 2, own_rows)
    mine = lax.all_gather(cotangent, SAME_CORE, axis=0, tiled=True)
    mine = mine.reshape(chips_x, group_tok, width)
    dims = (((1,), (1,)), ((0,), (0,)))
    cols_partner = jnp.take(columns, 1 - core, axis=2)
    cols_own = jnp.take(columns, core, axis=2)
    g_partner = lax.dot_general(
        cols_partner, mine, dims, preferred_element_type=jnp.float32
    ).astype(jnp.bfloat16)
    received = lax.ppermute(g_partner, "core", [(0, 1), (1, 0)])
    g_own = lax.dot_general(
        cols_own, mine, dims, preferred_element_type=jnp.float32
    ).astype(jnp.bfloat16)
    owned = jnp.concatenate([g_own, received])
    half = jnp.arange(chips_x, dtype=jnp.int32) * 2
    order = jnp.concatenate([half + core, half + 1 - core])
    keys = [(i, j) for i in range(groups) for j in range(i, groups)]
    partial = jnp.stack(
        [
            jnp.sum(owned[i].astype(jnp.float32) * owned[j].astype(jnp.float32), axis=1)
            for i, j in keys
        ]
    )
    sums = jnp.sum(partial, axis=1)
    ids = jnp.arange(groups, dtype=jnp.int32)
    pos = jnp.where(ids % 2 == core, ids // 2, chips_x + ids // 2)
    lo = jnp.minimum(pos[:, None], pos[None, :])
    hi = jnp.maximum(pos[:, None], pos[None, :])
    device_gram = jnp.take(sums, lo * groups - lo * (lo - 1) // 2 + (hi - lo))
    gram = device_gram
    for axes in (("core",), ("pair", "x"), ("fsdp",)):
        gram = lax.psum(gram, axes)
    score = jnp.sum(gram, axis=1) * (groups / jnp.trace(gram))
    onehot = (domain_ids[:, None] == jnp.arange(groups, dtype=jnp.int32)[None, :]).astype(
        jnp.float32
    )
    logits = log_weights + 2.0 * jnp.sum(onehot * score[:, None], axis=0)
    new_domain_weights = jax.nn.softmax(logits)
    group_w = jnp.sum(onehot * new_domain_weights[None, :], axis=1)
    local_w = jnp.take(group_w, order)
    steps_f = step_count[0].astype(jnp.float32)
    fix_one = 1.0 - jnp.exp(steps_f * jnp.log(jnp.float32(0.9)))
    fix_two = 1.0 - jnp.exp(steps_f * jnp.log(jnp.float32(0.95)))
    scal = jnp.concatenate([local_w, jnp.stack([fix_one, fix_two])])
    new_weight, new_moment, new_second = adam_update(scal, g_own, received, moment, second, weight)
    return (new_weight, new_moment, new_second, new_domain_weights)


def solution(mesh):
    chips = mesh.shape["dom"] // 2
    flat = Mesh(mesh.devices.reshape(chips, 2, mesh.shape["fsdp"] // 2, 2), FLAT)
    row = P(FLAT, None)
    return jax.shard_map(
        on_device,
        mesh=flat,
        in_specs=(row, row, row, row, row, P(), P(), P()),
        out_specs=(row, row, row, P()),
        check_vma=False,
    )
```

```python
import jax
import jax.numpy as jnp
from jax import lax
from jax.experimental import pallas as pl
from jax.experimental.pallas import tpu as pltpu
from jax.sharding import Mesh, PartitionSpec as P

FLAT = ("x", "core", "fsdp", "pair")
SAME_CORE = ("x", "fsdp", "pair")


def adam_kernel(scal_ref, own_ref, recv_ref, m_ref, s_ref, w_ref, nw_ref, nm_ref, ns_ref):
    half = own_ref.shape[0]
    combined = scal_ref[0] * own_ref[0].astype(jnp.float32)
    for k in range(1, half):
        combined = combined + scal_ref[k] * own_ref[k].astype(jnp.float32)
    for k in range(half):
        combined = combined + scal_ref[half + k] * recv_ref[k].astype(jnp.float32)
    fix_one = scal_ref[2 * half]
    fix_two = scal_ref[2 * half + 1]
    new_moment = 0.9 * m_ref[...] + 0.1 * combined
    new_second = 0.95 * s_ref[...] + 0.05 * combined * combined
    update = new_moment / fix_one / (jnp.sqrt(new_second / fix_two) + 1e-08)
    nw_ref[...] = (w_ref[...].astype(jnp.float32) - 0.002 * update).astype(nw_ref.dtype)
    nm_ref[...] = new_moment
    ns_ref[...] = new_second


def adam_update(scal, g_own, received, moment, second, weight):
    half, rows, width = g_own.shape
    tile = next(t for t in (112, 64, 32, 16, rows) if rows % t == 0)
    grad_spec = pl.BlockSpec((half, tile, width), lambda i: (0, i, 0))
    row_spec = pl.BlockSpec((tile, width), lambda i: (i, 0))
    elems = rows * width
    return pl.pallas_call(
        adam_kernel,
        grid=(rows // tile,),
        in_specs=[
            pl.BlockSpec(memory_space=pltpu.SMEM),
            grad_spec,
            grad_spec,
            row_spec,
            row_spec,
            row_spec,
        ],
        out_specs=[row_spec, row_spec, row_spec],
        out_shape=[
            jax.ShapeDtypeStruct((rows, width), weight.dtype),
            jax.ShapeDtypeStruct((rows, width), jnp.float32),
            jax.ShapeDtypeStruct((rows, width), jnp.float32),
        ],
        cost_estimate=pl.CostEstimate(
            flops=20 * elems, transcendentals=2 * elems, bytes_accessed=elems * (4 * half + 20)
        ),
    )(scal, g_own, received, moment, second, weight)


def on_device(acts, cotangent, weight, moment, second, log_weights, domain_ids, step_count):
    chips_x = lax.axis_size("x")
    members = lax.axis_size("fsdp") * lax.axis_size("pair")
    groups = chips_x * 2
    tok_rows = acts.shape[0]
    group_tok = members * tok_rows
    width = cotangent.shape[1]
    own_rows = weight.shape[0]
    core = lax.axis_index("core")
    shaped = acts.reshape(tok_rows, chips_x, 2, members, own_rows).transpose(0, 1, 3, 2, 4)
    shaped = shaped.reshape(tok_rows, chips_x * members, 2 * own_rows)
    columns = lax.all_to_all(shaped, SAME_CORE, split_axis=1, concat_axis=0, tiled=True)
    columns = columns.reshape(chips_x, group_tok, 2, own_rows)
    mine = lax.all_gather(cotangent, SAME_CORE, axis=0, tiled=True)
    mine = mine.reshape(chips_x, group_tok, width)
    dims = (((1,), (1,)), ((0,), (0,)))
    cols_partner = jnp.take(columns, 1 - core, axis=2)
    cols_own = jnp.take(columns, core, axis=2)
    dims = (((0,), (0,)), ((), ()))

    def grads(cols):
        return jnp.stack(
            [
                lax.dot_general(cols[x], mine[x], dims, preferred_element_type=jnp.float32)
                for x in range(chips_x)
            ]
        ).astype(jnp.bfloat16)

    g_partner = grads(cols_partner)
    received = lax.ppermute(g_partner, "core", [(0, 1), (1, 0)])
    g_own = grads(cols_own)
    owned = jnp.concatenate([g_own, received])
    half = jnp.arange(chips_x, dtype=jnp.int32) * 2
    order = jnp.concatenate([half + core, half + 1 - core])
    keys = [(i, j) for i in range(groups) for j in range(i, groups)]
    partial = jnp.stack(
        [
            jnp.sum(owned[i].astype(jnp.float32) * owned[j].astype(jnp.float32), axis=0)
            for i, j in keys
        ]
    )
    sums = jnp.sum(partial, axis=1)
    ids = jnp.arange(groups, dtype=jnp.int32)
    pos = jnp.where(ids % 2 == core, ids // 2, chips_x + ids // 2)
    lo = jnp.minimum(pos[:, None], pos[None, :])
    hi = jnp.maximum(pos[:, None], pos[None, :])
    device_gram = jnp.take(sums, lo * groups - lo * (lo - 1) // 2 + (hi - lo))
    gram = device_gram
    for axes in (("core",), ("pair", "x"), ("fsdp",)):
        gram = lax.psum(gram, axes)
    score = jnp.sum(gram, axis=1) * (groups / jnp.trace(gram))
    onehot = (domain_ids[:, None] == jnp.arange(groups, dtype=jnp.int32)[None, :]).astype(
        jnp.float32
    )
    logits = log_weights + 2.0 * jnp.sum(onehot * score[:, None], axis=0)
    new_domain_weights = jax.nn.softmax(logits)
    group_w = jnp.sum(onehot * new_domain_weights[None, :], axis=1)
    local_w = jnp.take(group_w, order)
    steps_f = step_count[0].astype(jnp.float32)
    fix_one = 1.0 - jnp.exp(steps_f * jnp.log(jnp.float32(0.9)))
    fix_two = 1.0 - jnp.exp(steps_f * jnp.log(jnp.float32(0.95)))
    scal = jnp.concatenate([local_w, jnp.stack([fix_one, fix_two])])
    new_weight, new_moment, new_second = adam_update(scal, g_own, received, moment, second, weight)
    return (new_weight, new_moment, new_second, new_domain_weights)


def solution(mesh):
    chips = mesh.shape["dom"] // 2
    flat = Mesh(mesh.devices.reshape(chips, 2, mesh.shape["fsdp"] // 2, 2), FLAT)
    row = P(FLAT, None)
    return jax.shard_map(
        on_device,
        mesh=flat,
        in_specs=(row, row, row, row, row, P(), P(), P()),
        out_specs=(row, row, row, P()),
        check_vma=False,
    )
```

```python
import jax
import jax.numpy as jnp
from jax import lax
from jax.experimental import pallas as pl
from jax.experimental.pallas import tpu as pltpu
from jax.sharding import Mesh, PartitionSpec as P

FLAT = ("x", "core", "fsdp", "pair")
SAME_CORE = ("x", "fsdp", "pair")


def adam_kernel(scal_ref, own_ref, recv_ref, m_ref, s_ref, w_ref, nw_ref, nm_ref, ns_ref):
    half = own_ref.shape[0]
    combined = scal_ref[0] * own_ref[0].astype(jnp.float32)
    for k in range(1, half):
        combined = combined + scal_ref[k] * own_ref[k].astype(jnp.float32)
    for k in range(half):
        combined = combined + scal_ref[half + k] * recv_ref[k].astype(jnp.float32)
    fix_one = scal_ref[2 * half]
    fix_two = scal_ref[2 * half + 1]
    new_moment = 0.9 * m_ref[...] + 0.1 * combined
    new_second = 0.95 * s_ref[...] + 0.05 * combined * combined
    update = new_moment / fix_one / (jnp.sqrt(new_second / fix_two) + 1e-08)
    nw_ref[...] = (w_ref[...].astype(jnp.float32) - 0.002 * update).astype(nw_ref.dtype)
    nm_ref[...] = new_moment
    ns_ref[...] = new_second


def adam_update(scal, g_own, received, moment, second, weight):
    half, rows, width = g_own.shape
    tile = next(t for t in (112, 64, 32, 16, rows) if rows % t == 0)
    grad_spec = pl.BlockSpec((half, tile, width), lambda i: (0, i, 0))
    row_spec = pl.BlockSpec((tile, width), lambda i: (i, 0))
    elems = rows * width
    return pl.pallas_call(
        adam_kernel,
        grid=(rows // tile,),
        in_specs=[
            pl.BlockSpec(memory_space=pltpu.SMEM),
            grad_spec,
            grad_spec,
            row_spec,
            row_spec,
            row_spec,
        ],
        out_specs=[row_spec, row_spec, row_spec],
        out_shape=[
            jax.ShapeDtypeStruct((rows, width), weight.dtype),
            jax.ShapeDtypeStruct((rows, width), jnp.float32),
            jax.ShapeDtypeStruct((rows, width), jnp.float32),
        ],
        cost_estimate=pl.CostEstimate(
            flops=20 * elems, transcendentals=2 * elems, bytes_accessed=elems * (4 * half + 20)
        ),
    )(scal, g_own, received, moment, second, weight)


def on_device(acts, cotangent, weight, moment, second, log_weights, domain_ids, step_count):
    chips_x = lax.axis_size("x")
    members = lax.axis_size("fsdp") * lax.axis_size("pair")
    groups = chips_x * 2
    tok_rows = acts.shape[0]
    group_tok = members * tok_rows
    width = cotangent.shape[1]
    own_rows = weight.shape[0]
    core = lax.axis_index("core")
    shaped = acts.reshape(tok_rows, chips_x, 2, members, own_rows).transpose(0, 1, 3, 2, 4)
    shaped = shaped.reshape(tok_rows, chips_x * members, 2 * own_rows)
    columns = lax.all_to_all(shaped, SAME_CORE, split_axis=1, concat_axis=0, tiled=True)
    columns = columns.reshape(chips_x, group_tok, 2, own_rows)
    mine = lax.all_gather(cotangent, SAME_CORE, axis=0, tiled=True)
    mine = mine.reshape(chips_x, group_tok, width)
    dims = (((1,), (1,)), ((0,), (0,)))
    cols_partner = jnp.take(columns, 1 - core, axis=2)
    cols_own = jnp.take(columns, core, axis=2)
    g_partner = lax.dot_general(
        cols_partner, mine, dims, preferred_element_type=jnp.float32
    ).astype(jnp.bfloat16)
    received = lax.ppermute(g_partner, "core", [(0, 1), (1, 0)])
    g_own = lax.dot_general(
        cols_own, mine, dims, preferred_element_type=jnp.float32
    ).astype(jnp.bfloat16)
    owned = jnp.concatenate([g_own, received])
    half = jnp.arange(chips_x, dtype=jnp.int32) * 2
    order = jnp.concatenate([half + core, half + 1 - core])
    keys = [(i, j) for i in range(groups) for j in range(i, groups)]
    partial = jnp.stack(
        [
            jnp.sum(
                (owned[i].astype(jnp.float32) * owned[j].astype(jnp.float32)).reshape(
                    own_rows // 8, 8, width
                ),
                axis=0,
            )
            for i, j in keys
        ]
    )
    sums = jnp.sum(lax.optimization_barrier(partial), axis=(1, 2))
    ids = jnp.arange(groups, dtype=jnp.int32)
    pos = jnp.where(ids % 2 == core, ids // 2, chips_x + ids // 2)
    lo = jnp.minimum(pos[:, None], pos[None, :])
    hi = jnp.maximum(pos[:, None], pos[None, :])
    device_gram = jnp.take(sums, lo * groups - lo * (lo - 1) // 2 + (hi - lo))
    gram = device_gram
    for axes in (("core",), ("pair", "x"), ("fsdp",)):
        gram = lax.psum(gram, axes)
    score = jnp.sum(gram, axis=1) * (groups / jnp.trace(gram))
    onehot = (domain_ids[:, None] == jnp.arange(groups, dtype=jnp.int32)[None, :]).astype(
        jnp.float32
    )
    logits = log_weights + 2.0 * jnp.sum(onehot * score[:, None], axis=0)
    new_domain_weights = jax.nn.softmax(logits)
    group_w = jnp.sum(onehot * new_domain_weights[None, :], axis=1)
    local_w = jnp.take(group_w, order)
    steps_f = step_count[0].astype(jnp.float32)
    fix_one = 1.0 - jnp.exp(steps_f * jnp.log(jnp.float32(0.9)))
    fix_two = 1.0 - jnp.exp(steps_f * jnp.log(jnp.float32(0.95)))
    scal = jnp.concatenate([local_w, jnp.stack([fix_one, fix_two])])
    new_weight, new_moment, new_second = adam_update(scal, g_own, received, moment, second, weight)
    return (new_weight, new_moment, new_second, new_domain_weights)


def solution(mesh):
    chips = mesh.shape["dom"] // 2
    flat = Mesh(mesh.devices.reshape(chips, 2, mesh.shape["fsdp"] // 2, 2), FLAT)
    row = P(FLAT, None)
    return jax.shard_map(
        on_device,
        mesh=flat,
        in_specs=(row, row, row, row, row, P(), P(), P()),
        out_specs=(row, row, row, P()),
        check_vma=False,
    )
```

```python
import jax
import jax.numpy as jnp
from jax import lax
from jax.experimental import pallas as pl
from jax.experimental.pallas import tpu as pltpu
from jax.sharding import Mesh, PartitionSpec as P

FLAT = ("x", "core", "fsdp", "pair")
SAME_CORE = ("x", "fsdp", "pair")


def adam_kernel(scal_ref, own_ref, recv_ref, m_ref, s_ref, w_ref, nw_ref, nm_ref, ns_ref):
    half = own_ref.shape[0]
    combined = scal_ref[0] * own_ref[0].astype(jnp.float32)
    for k in range(1, half):
        combined = combined + scal_ref[k] * own_ref[k].astype(jnp.float32)
    for k in range(half):
        combined = combined + scal_ref[half + k] * recv_ref[k].astype(jnp.float32)
    fix_one = scal_ref[2 * half]
    fix_two = scal_ref[2 * half + 1]
    new_moment = 0.9 * m_ref[...] + 0.1 * combined
    new_second = 0.95 * s_ref[...] + 0.05 * combined * combined
    update = new_moment / fix_one / (jnp.sqrt(new_second / fix_two) + 1e-08)
    nw_ref[...] = (w_ref[...].astype(jnp.float32) - 0.002 * update).astype(nw_ref.dtype)
    nm_ref[...] = new_moment
    ns_ref[...] = new_second


def adam_update(scal, g_own, received, moment, second, weight):
    half, rows, width = g_own.shape
    tile = next(t for t in (112, 64, 32, 16, rows) if rows % t == 0)
    grad_spec = pl.BlockSpec((half, tile, width), lambda i: (0, i, 0))
    row_spec = pl.BlockSpec((tile, width), lambda i: (i, 0))
    elems = rows * width
    return pl.pallas_call(
        adam_kernel,
        grid=(rows // tile,),
        in_specs=[
            pl.BlockSpec(memory_space=pltpu.SMEM),
            grad_spec,
            grad_spec,
            row_spec,
            row_spec,
            row_spec,
        ],
        out_specs=[row_spec, row_spec, row_spec],
        out_shape=[
            jax.ShapeDtypeStruct((rows, width), weight.dtype),
            jax.ShapeDtypeStruct((rows, width), jnp.float32),
            jax.ShapeDtypeStruct((rows, width), jnp.float32),
        ],
        cost_estimate=pl.CostEstimate(
            flops=20 * elems, transcendentals=2 * elems, bytes_accessed=elems * (4 * half + 20)
        ),
    )(scal, g_own, received, moment, second, weight)


def on_device(acts, cotangent, weight, moment, second, log_weights, domain_ids, step_count):
    chips_x = lax.axis_size("x")
    members = lax.axis_size("fsdp") * lax.axis_size("pair")
    groups = chips_x * 2
    tok_rows = acts.shape[0]
    group_tok = members * tok_rows
    width = cotangent.shape[1]
    own_rows = weight.shape[0]
    core = lax.axis_index("core")
    shaped = acts.reshape(tok_rows, chips_x, 2, members, own_rows).transpose(0, 1, 3, 2, 4)
    shaped = shaped.reshape(tok_rows, chips_x * members, 2 * own_rows)
    columns = lax.all_to_all(shaped, SAME_CORE, split_axis=1, concat_axis=0, tiled=True)
    columns = columns.reshape(chips_x, group_tok, 2, own_rows)
    mine = lax.all_gather(cotangent, SAME_CORE, axis=0, tiled=True)
    mine = mine.reshape(chips_x, group_tok, width)
    dims = (((1,), (1,)), ((0,), (0,)))
    cols_partner = jnp.take(columns, 1 - core, axis=2)
    cols_own = jnp.take(columns, core, axis=2)
    g_partner = lax.dot_general(
        cols_partner, mine, dims, preferred_element_type=jnp.float32
    ).astype(jnp.bfloat16)
    received = lax.ppermute(g_partner, "core", [(0, 1), (1, 0)])
    g_own = lax.dot_general(
        cols_own, mine, dims, preferred_element_type=jnp.float32
    ).astype(jnp.bfloat16)
    owned = jnp.concatenate([g_own, received])
    half = jnp.arange(chips_x, dtype=jnp.int32) * 2
    order = jnp.concatenate([half + core, half + 1 - core])
    keys = [(i, j) for i in range(groups) for j in range(i, groups)]
    partial = jnp.stack(
        [
            jnp.sum(
                (owned[i].astype(jnp.float32) * owned[j].astype(jnp.float32)).reshape(
                    own_rows // 8, 8, width
                ),
                axis=0,
            )
            for i, j in keys
        ]
    )
    sums = jnp.sum(lax.optimization_barrier(partial), axis=(1, 2))
    ids = jnp.arange(groups, dtype=jnp.int32)
    pos = jnp.where(ids % 2 == core, ids // 2, chips_x + ids // 2)
    lo = jnp.minimum(pos[:, None], pos[None, :])
    hi = jnp.maximum(pos[:, None], pos[None, :])
    device_gram = jnp.take(sums, lo * groups - lo * (lo - 1) // 2 + (hi - lo))
    gram = device_gram
    for axes in (("core",), ("x",), ("fsdp", "pair")):
        gram = lax.psum(gram, axes)
    score = jnp.sum(gram, axis=1) * (groups / jnp.trace(gram))
    onehot = (domain_ids[:, None] == jnp.arange(groups, dtype=jnp.int32)[None, :]).astype(
        jnp.float32
    )
    logits = log_weights + 2.0 * jnp.sum(onehot * score[:, None], axis=0)
    new_domain_weights = jax.nn.softmax(logits)
    group_w = jnp.sum(onehot * new_domain_weights[None, :], axis=1)
    local_w = jnp.take(group_w, order)
    steps_f = step_count[0].astype(jnp.float32)
    fix_one = 1.0 - jnp.exp(steps_f * jnp.log(jnp.float32(0.9)))
    fix_two = 1.0 - jnp.exp(steps_f * jnp.log(jnp.float32(0.95)))
    scal = jnp.concatenate([local_w, jnp.stack([fix_one, fix_two])])
    new_weight, new_moment, new_second = adam_update(scal, g_own, received, moment, second, weight)
    return (new_weight, new_moment, new_second, new_domain_weights)


def solution(mesh):
    chips = mesh.shape["dom"] // 2
    flat = Mesh(mesh.devices.reshape(chips, 2, mesh.shape["fsdp"] // 2, 2), FLAT)
    row = P(FLAT, None)
    return jax.shard_map(
        on_device,
        mesh=flat,
        in_specs=(row, row, row, row, row, P(), P(), P()),
        out_specs=(row, row, row, P()),
        check_vma=False,
    )
```
